32 devices in a mesh: row: 8 (over z, y), col: 4 (over x, core).
Axes of the slice: x: 2, y: 2, z: 4, core: 2. Of those that a mesh axis runs over, the one named last changes fastest.
Arguments:
- gram: float32 [16384, 16384], P('row', 'col'), may hold values from -1 to 17, as said below
Outputs:
- factored: float32 [16384, 16384], P('row', 'col')
The draws below stay inside these ranges and needn't reach their ends.
Inputs may be any that keep to these rules, and one draw needn't show every extreme that they name: gram holds a symmetric positive definite matrix in the block-cyclic order of the steps.
All inputs are finite; a program needn't handle non-finite values.
Results may differ from the reference program's by a relative error of at most 0.0001.
Values sent between devices are 32-bit elements; how exact they have to be, the bound alone decides.
No kernel may reach another device: no remote copies, remote signals or barrier semaphores. Data moves between devices by JAX's collectives and lax.ppermute only.
A program may use at most 192 MiB of HBM per device.

```python
import math
import jax
import jax.numpy as jnp
from jax import lax

M = 16384
NB = 512
STEPS = 2
PROW = 8
PCOL = 4
MB = 256
LR = 8
LC = 8


def draw_gram(key, part):
    base_key = jax.random.fold_in(key, 7)
    key_points, key_noise, key_scale = jax.random.split(base_key, 3)
    points = jax.random.uniform(key_points, (M, 3), jnp.float32)
    scales = jnp.exp(jax.random.uniform(key_scale, (M,), jnp.float32, 0.0, math.log(3.2)))
    distance = jnp.zeros((M, M), jnp.float32)
    for coord in range(3):
        gap = points[:, coord][:, None] - points[:, coord][None, :]
        distance = distance + gap * gap
    kernel = jnp.exp(-jnp.sqrt(distance) * 2.0)
    noise = jax.random.uniform(key_noise, (M, M), jnp.float32, -1.0, 1.0)
    noise = (noise + noise.T) * 0.5
    matrix = 0.02 * kernel + 0.5 / math.sqrt(M) * noise + jnp.eye(M, dtype=jnp.float32)
    matrix = scales[:, None] * matrix * scales[None, :]
    return matrix.reshape(LR, PROW, MB, LC, PCOL, NB).transpose(1, 0, 2, 4, 3, 5).reshape(M, M)


def setup_inputs(seed: int = 0) -> dict:
    key_of = jax.random.split(jax.random.key(seed), 2)
    gram = draw_gram(jax.random.fold_in(key_of[1], 71), 0)
    return dict(gram=gram)


def to_natural(stored):
    return stored.reshape(PROW, LR, MB, PCOL, LC, NB).transpose(1, 0, 2, 4, 3, 5).reshape(M, M)

def to_stored(matrix):
    return matrix.reshape(LR, PROW, MB, LC, PCOL, NB).transpose(1, 0, 2, 4, 3, 5).reshape(M, M)

def factor_panel(matrix, panel_index):
    first_row = panel_index * NB
    end_row = first_row + NB
    low_factor = jnp.linalg.cholesky(matrix[first_row:end_row, first_row:end_row])
    below = jax.scipy.linalg.solve_triangular(low_factor, matrix[end_row:, first_row:end_row].T, lower=True).T
    column = jnp.concatenate([jnp.zeros((first_row, NB), jnp.float32), low_factor, below], axis=0)
    return (matrix.at[:, first_row:end_row].set(column), below)

def reference(gram):
    matrix = to_natural(gram)
    for panel_index in range(STEPS):
        first_row = panel_index * NB
        end_row = first_row + NB
        matrix, below = factor_panel(matrix, panel_index)
        product = jnp.dot(below.astype(jnp.float32), below.T.astype(jnp.float32), precision=lax.Precision.HIGHEST, preferred_element_type=jnp.float32)
        matrix = matrix.at[end_row:, end_row:].set(matrix[end_row:, end_row:] - product)
        matrix = matrix.at[first_row:end_row, end_row:].set(0.0)
    matrix, below = factor_panel(matrix, STEPS)
    return to_stored(matrix)
```

```python
import jax
import jax.numpy as jnp
from jax import lax
from jax.sharding import PartitionSpec as P

NB = 512
STEPS = 2


def from_partner(block, axis, apart):
    count = lax.axis_size(axis)
    route = []
    for low in range(count):
        high = low | 1 << apart
        if high != low and high < count:
            route += [(low, high), (high, low)]
    return lax.ppermute(block, axis, route)


def global_index(count, block, grid, position):
    ladder = jnp.arange(count, dtype=jnp.int32)
    return (ladder // block * grid + position) * block + ladder % block


def times_transposed(left, right):
    return lax.dot_general(
        left,
        right,
        (((1,), (1,)), ((), ())),
        precision=lax.Precision.HIGHEST,
        preferred_element_type=jnp.float32,
    )


def bcast_col(value, owner, col_id, grid_cols):
    held = value
    have = [owner]
    bit = 1
    while bit < grid_cols:
        route = [(h, h ^ bit) for h in have if (h ^ bit) < grid_cols]
        got = lax.ppermute(held, "col", route)
        targets = [t for _, t in route]
        is_target = jnp.zeros((), bool)
        for t in targets:
            is_target = is_target | (col_id == t)
        held = jnp.where(is_target, got, held)
        have = have + targets
        bit <<= 1
    return held


def local(gram):
    grid_rows = lax.axis_size("row")
    grid_cols = lax.axis_size("col")
    row_id = lax.axis_index("row")
    col_id = lax.axis_index("col")
    rblock = NB * grid_cols // grid_rows
    per_class = grid_rows // grid_cols
    panels = STEPS + 1
    assert panels <= grid_cols and panels * per_class <= grid_rows
    local_rows = gram.shape[0]
    local_cols = gram.shape[1]
    blocks = local_rows // rblock
    grows = global_index(local_rows, rblock, grid_rows, row_id)
    gcols = global_index(local_cols, NB, grid_cols, col_id)
    row_class = row_id // per_class
    identity = jnp.eye(NB, dtype=jnp.float32)

    tile = gram[0:rblock, 0:NB]
    colblk = lax.all_gather(tile, "row", axis=0, tiled=True)
    colblk = colblk[: panels * NB].reshape(panels, NB, NB)
    send_a = jnp.where(col_id == 0, colblk[0], colblk[1])
    recv_a = lax.ppermute(send_a, "col", [(0, 1), (1, 2)])
    recv_b = lax.ppermute(colblk[0:2], "col", [(0, 2)])

    def pick(options, default):
        out = default
        for col, val in options:
            out = jnp.where(col_id == col, val, out)
        return out

    g00 = pick([(0, colblk[0]), (1, recv_a), (2, recv_b[0])], identity)
    g10 = pick([(1, colblk[0].T), (2, recv_b[1])], jnp.zeros_like(identity))
    g11 = pick([(1, colblk[1]), (2, recv_a)], identity)
    g20 = pick([(2, colblk[0].T)], jnp.zeros_like(identity))
    g21 = pick([(2, colblk[1].T)], jnp.zeros_like(identity))
    g22 = pick([(2, colblk[2])], identity)

    def factor(diag):
        low_factor = jnp.linalg.cholesky(diag)
        inverse = jax.scipy.linalg.solve_triangular(low_factor, identity, lower=True)
        return low_factor, inverse

    panel_in = gram[:, 0:NB]

    def panel_rows(updated, low_factor, inverse, panel_index):
        end_row = panel_index * NB + NB
        solved = times_transposed(updated, inverse)
        trailing = jnp.where((grows >= end_row)[:, None], solved, 0.0)
        first = panel_index * per_class
        member = jnp.clip(row_id - first, 0, per_class - 1)
        rows_diag = lax.dynamic_slice_in_dim(low_factor, member * rblock, rblock, 0)
        in_panel = (row_id >= first) & (row_id < first + per_class)
        patched = jnp.where(in_panel, rows_diag, trailing[0:rblock])
        column = trailing.at[0:rblock].set(patched)
        return trailing, column

    def spread_columns_of(spread_rows_all):
        pieces = spread_rows_all.reshape(grid_cols, blocks // grid_cols * rblock, NB)
        shift_bits = per_class.bit_length() - 1
        for bit_level in reversed(range(grid_cols.bit_length() - 1)):
            halfway = pieces.shape[0] // 2
            own_bit = row_class >> bit_level & 1
            wanted = col_id >> bit_level & 1
            upper = own_bit == 1
            retained = jnp.where(upper, pieces[halfway:], pieces[:halfway])
            outgoing = jnp.where(upper, pieces[:halfway], pieces[halfway:])
            received = from_partner(outgoing, "row", shift_bits + bit_level)
            pieces = jnp.where(own_bit == wanted, retained, received)
        gathered = lax.all_gather(pieces[0], "row", axis=0, tiled=True)
        spread = gathered.reshape(grid_cols, per_class, blocks // grid_cols, rblock, NB)
        return jnp.transpose(spread, (0, 2, 1, 3, 4)).reshape(local_cols, NB)

    l0, i0 = factor(g00)
    l0_b1 = times_transposed(g10, i0)
    l0_b2 = times_transposed(g20, i0)
    trail0, column0 = panel_rows(panel_in, l0, i0, 0)
    rows0 = bcast_col(trail0, 0, col_id, grid_cols)
    cols0 = spread_columns_of(rows0)

    l1, i1 = factor(g11 - times_transposed(l0_b1, l0_b1))
    l1_b2 = times_transposed(g21 - times_transposed(l0_b2, l0_b1), i1)
    upd1 = panel_in - times_transposed(rows0, l0_b1)
    trail1, column1 = panel_rows(upd1, l1, i1, 1)
    rows1 = bcast_col(trail1, 1, col_id, grid_cols)
    cols1 = spread_columns_of(rows1)

    d2 = g22 - times_transposed(l0_b2, l0_b2) - times_transposed(l1_b2, l1_b2)
    l2, i2 = factor(d2)
    upd2 = panel_in - times_transposed(rows0, l0_b2) - times_transposed(rows1, l1_b2)
    _, column2 = panel_rows(upd2, l2, i2, 2)

    left = jnp.concatenate([rows0, rows1], axis=1)
    right = jnp.concatenate([cols0, cols1], axis=1)
    updated = gram - times_transposed(left, right)
    in_steps = grows < STEPS * NB
    panel_end = (grows // NB + 1) * NB
    zero = in_steps[:, None] & (gcols[None, :] >= panel_end[:, None])
    updated = jnp.where(zero, 0.0, updated)
    own_column = pick([(0, column0), (1, column1), (2, column2)], updated[:, 0:NB])
    updated = updated.at[:, 0:NB].set(own_column)
    return updated


def solution(mesh):
    placed = (P("row", "col"),)
    return jax.shard_map(
        local, mesh=mesh, in_specs=placed, out_specs=P("row", "col"), check_vma=False
    )
```

```python
import jax
import jax.numpy as jnp
from jax import lax
from jax.sharding import PartitionSpec as P

NB = 512
STEPS = 2


def global_index(count, block, grid, position):
    ladder = jnp.arange(count, dtype=jnp.int32)
    return (ladder // block * grid + position) * block + ladder % block


def times_transposed(left, right, precision=lax.Precision.HIGHEST):
    return lax.dot_general(
        left,
        right,
        (((1,), (1,)), ((), ())),
        precision=precision,
        preferred_element_type=jnp.float32,
    )


def bcast_col(value, owner, col_id, grid_cols):
    held = value
    have = [owner]
    bit = 1
    while bit < grid_cols:
        route = [(h, h ^ bit) for h in have if (h ^ bit) < grid_cols]
        got = lax.ppermute(held, "col", route)
        targets = [t for _, t in route]
        is_target = jnp.zeros((), bool)
        for t in targets:
            is_target = is_target | (col_id == t)
        held = jnp.where(is_target, got, held)
        have = have + targets
        bit <<= 1
    return held


def local(gram):
    grid_rows = lax.axis_size("row")
    grid_cols = lax.axis_size("col")
    row_id = lax.axis_index("row")
    col_id = lax.axis_index("col")
    rblock = NB * grid_cols // grid_rows
    per_class = grid_rows // grid_cols
    panels = STEPS + 1
    assert panels <= grid_cols and panels * per_class <= grid_rows
    local_rows = gram.shape[0]
    local_cols = gram.shape[1]
    blocks = local_rows // rblock
    grows = global_index(local_rows, rblock, grid_rows, row_id)
    gcols = global_index(local_cols, NB, grid_cols, col_id)
    row_class = row_id // per_class
    identity = jnp.eye(NB, dtype=jnp.float32)

    tile = gram[0:rblock, 0:NB]
    colblk = lax.all_gather(tile, "row", axis=0, tiled=True)
    colblk = colblk[: panels * NB].reshape(panels, NB, NB)
    send_a = jnp.where(col_id == 0, colblk[0], colblk[1])
    recv_a = lax.ppermute(send_a, "col", [(0, 1), (1, 2)])
    recv_b = lax.ppermute(colblk[0:2], "col", [(0, 2)])

    def pick(options, default):
        out = default
        for col, val in options:
            out = jnp.where(col_id == col, val, out)
        return out

    g00 = pick([(0, colblk[0]), (1, recv_a), (2, recv_b[0])], identity)
    g10 = pick([(1, colblk[0].T), (2, recv_b[1])], jnp.zeros_like(identity))
    g11 = pick([(1, colblk[1]), (2, recv_a)], identity)
    g20 = pick([(2, colblk[0].T)], jnp.zeros_like(identity))
    g21 = pick([(2, colblk[1].T)], jnp.zeros_like(identity))
    g22 = pick([(2, colblk[2])], identity)

    def factor(diag):
        low_factor = jnp.linalg.cholesky(diag)
        inverse = jax.scipy.linalg.solve_triangular(low_factor, identity, lower=True)
        return low_factor, inverse

    panel_in = gram[:, 0:NB]

    def panel_rows(updated, low_factor, inverse, panel_index):
        end_row = panel_index * NB + NB
        solved = times_transposed(updated, inverse)
        trailing = jnp.where((grows >= end_row)[:, None], solved, 0.0)
        first = panel_index * per_class
        member = jnp.clip(row_id - first, 0, per_class - 1)
        rows_diag = lax.dynamic_slice_in_dim(low_factor, member * rblock, rblock, 0)
        in_panel = (row_id >= first) & (row_id < first + per_class)
        patched = jnp.where(in_panel, rows_diag, trailing[0:rblock])
        column = trailing.at[0:rblock].set(patched)
        return trailing, column

    def spread_columns_of(trail, owner):
        span = blocks // grid_cols * rblock
        pieces = trail.reshape(grid_cols, span, NB)
        got = pieces[0]
        for piece in range(grid_cols):
            route = []
            for source_row in range(grid_rows):
                target_row = piece * per_class + source_row % per_class
                target_col = source_row // per_class
                route.append((source_row * grid_cols + owner, target_row * grid_cols + target_col))
            received = lax.ppermute(pieces[piece], ("row", "col"), route)
            got = jnp.where(row_id // per_class == piece, received, got)
        gathered = lax.all_gather(got, "row", axis=0, tiled=True)
        spread = gathered.reshape(grid_cols, per_class, blocks // grid_cols, rblock, NB)
        return jnp.transpose(spread, (0, 2, 1, 3, 4)).reshape(local_cols, NB)

    l0, i0 = factor(g00)
    l0_b1 = times_transposed(g10, i0)
    l0_b2 = times_transposed(g20, i0)
    trail0, column0 = panel_rows(panel_in, l0, i0, 0)
    rows0 = bcast_col(trail0, 0, col_id, grid_cols)
    cols0 = spread_columns_of(trail0, 0)

    l1, i1 = factor(g11 - times_transposed(l0_b1, l0_b1))
    l1_b2 = times_transposed(g21 - times_transposed(l0_b2, l0_b1), i1)
    upd1 = panel_in - times_transposed(rows0, l0_b1)
    trail1, column1 = panel_rows(upd1, l1, i1, 1)
    rows1 = bcast_col(trail1, 1, col_id, grid_cols)
    cols1 = spread_columns_of(trail1, 1)

    d2 = g22 - times_transposed(l0_b2, l0_b2) - times_transposed(l1_b2, l1_b2)
    l2, i2 = factor(d2)
    upd2 = panel_in - times_transposed(rows0, l0_b2) - times_transposed(rows1, l1_b2)
    _, column2 = panel_rows(upd2, l2, i2, 2)

    left = jnp.concatenate([rows0, rows1], axis=1)
    right = jnp.concatenate([cols0, cols1], axis=1)
    updated = gram - times_transposed(left, right, lax.Precision.HIGH)
    in_steps = grows < STEPS * NB
    panel_end = (grows // NB + 1) * NB
    zero = in_steps[:, None] & (gcols[None, :] >= panel_end[:, None])
    updated = jnp.where(zero, 0.0, updated)
    own_column = pick([(0, column0), (1, column1), (2, column2)], updated[:, 0:NB])
    updated = updated.at[:, 0:NB].set(own_column)
    return updated


def solution(mesh):
    placed = (P("row", "col"),)
    return jax.shard_map(
        local, mesh=mesh, in_specs=placed, out_specs=P("row", "col"), check_vma=False
    )
```

```python
import jax
import jax.numpy as jnp
from jax import lax
from jax.sharding import PartitionSpec as P

NB = 512
STEPS = 2
SUB = 128


def global_index(count, block, grid, position):
    ladder = jnp.arange(count, dtype=jnp.int32)
    return (ladder // block * grid + position) * block + ladder % block


def times_transposed(left, right, precision=lax.Precision.HIGHEST):
    return lax.dot_general(
        left,
        right,
        (((1,), (1,)), ((), ())),
        precision=precision,
        preferred_element_type=jnp.float32,
    )


def bcast_col(value, owner, col_id, grid_cols):
    held = value
    have = [owner]
    bit = 1
    while bit < grid_cols:
        route = [(h, h ^ bit) for h in have if (h ^ bit) < grid_cols]
        got = lax.ppermute(held, "col", route)
        targets = [t for _, t in route]
        is_target = jnp.zeros((), bool)
        for t in targets:
            is_target = is_target | (col_id == t)
        held = jnp.where(is_target, got, held)
        have = have + targets
        bit <<= 1
    return held


def local(gram):
    grid_rows = lax.axis_size("row")
    grid_cols = lax.axis_size("col")
    row_id = lax.axis_index("row")
    col_id = lax.axis_index("col")
    rblock = NB * grid_cols // grid_rows
    per_class = grid_rows // grid_cols
    panels = STEPS + 1
    assert panels <= grid_cols and panels * per_class <= grid_rows
    local_rows = gram.shape[0]
    local_cols = gram.shape[1]
    blocks = local_rows // rblock
    grows = global_index(local_rows, rblock, grid_rows, row_id)
    gcols = global_index(local_cols, NB, grid_cols, col_id)
    row_class = row_id // per_class
    identity = jnp.eye(NB, dtype=jnp.float32)

    tile = gram[0:rblock, 0:NB]
    colblk = lax.all_gather(tile, "row", axis=0, tiled=True)
    colblk = colblk[: panels * NB].reshape(panels, NB, NB)
    send_a = jnp.where(col_id == 0, colblk[0], colblk[1])
    recv_a = lax.ppermute(send_a, "col", [(0, 1), (1, 2)])
    recv_b = lax.ppermute(colblk[0:2], "col", [(0, 2)])

    def pick(options, default):
        out = default
        for col, val in options:
            out = jnp.where(col_id == col, val, out)
        return out

    g00 = pick([(0, colblk[0]), (1, recv_a), (2, recv_b[0])], identity)
    g10 = pick([(1, colblk[0].T), (2, recv_b[1])], jnp.zeros_like(identity))
    g11 = pick([(1, colblk[1]), (2, recv_a)], identity)
    g20 = pick([(2, colblk[0].T)], jnp.zeros_like(identity))
    g21 = pick([(2, colblk[1].T)], jnp.zeros_like(identity))
    g22 = pick([(2, colblk[2])], identity)

    def factor(diag):
        sym = (diag + diag.T) * 0.5
        side = SUB
        count = NB // side
        eye_sub = jnp.eye(side, dtype=jnp.float32)
        diag_factors = []
        diag_inverses = []
        below_blocks = []
        rest = sym
        for step in range(count):
            lead = rest[0:side, 0:side]
            low = jnp.linalg.cholesky(lead)
            inv = jax.scipy.linalg.solve_triangular(low, eye_sub, lower=True)
            diag_factors.append(low)
            diag_inverses.append(inv)
            if step + 1 < count:
                below = times_transposed(rest[side:, 0:side], inv)
                below_blocks.append(below)
                rest = rest[side:, side:] - times_transposed(below, below)
        low_factor = jnp.zeros((NB, NB), jnp.float32)
        for step in range(count):
            at = step * side
            low_factor = low_factor.at[at : at + side, at : at + side].set(diag_factors[step])
            if step + 1 < count:
                low_factor = low_factor.at[at + side :, at : at + side].set(below_blocks[step])

        def invert(first, size):
            if size == side:
                return diag_inverses[first // side]
            half = size // 2
            top = invert(first, half)
            bottom = invert(first + half, half)
            corner = low_factor[first + half : first + size, first : first + half]
            mixed = -jnp.dot(bottom, jnp.dot(corner, top, precision=lax.Precision.HIGHEST),
                             precision=lax.Precision.HIGHEST)
            upper = jnp.concatenate([top, jnp.zeros((half, half), jnp.float32)], axis=1)
            lower = jnp.concatenate([mixed, bottom], axis=1)
            return jnp.concatenate([upper, lower], axis=0)

        return low_factor, invert(0, NB)

    panel_in = gram[:, 0:NB]

    def panel_rows(updated, low_factor, inverse, panel_index):
        end_row = panel_index * NB + NB
        solved = times_transposed(updated, inverse)
        trailing = jnp.where((grows >= end_row)[:, None], solved, 0.0)
        first = panel_index * per_class
        member = jnp.clip(row_id - first, 0, per_class - 1)
        rows_diag = lax.dynamic_slice_in_dim(low_factor, member * rblock, rblock, 0)
        in_panel = (row_id >= first) & (row_id < first + per_class)
        patched = jnp.where(in_panel, rows_diag, trailing[0:rblock])
        column = trailing.at[0:rblock].set(patched)
        return trailing, column

    def spread_columns_of(trail, owner):
        span = blocks // grid_cols * rblock
        pieces = trail.reshape(grid_cols, span, NB)
        got = pieces[0]
        for piece in range(grid_cols):
            route = []
            for source_row in range(grid_rows):
                target_row = piece * per_class + source_row % per_class
                target_col = source_row // per_class
                route.append((source_row * grid_cols + owner, target_row * grid_cols + target_col))
            received = lax.ppermute(pieces[piece], ("row", "col"), route)
            got = jnp.where(row_id // per_class == piece, received, got)
        gathered = lax.all_gather(got, "row", axis=0, tiled=True)
        spread = gathered.reshape(grid_cols, per_class, blocks // grid_cols, rblock, NB)
        return jnp.transpose(spread, (0, 2, 1, 3, 4)).reshape(local_cols, NB)

    l0, i0 = factor(g00)
    l0_b1 = times_transposed(g10, i0)
    l0_b2 = times_transposed(g20, i0)
    trail0, column0 = panel_rows(panel_in, l0, i0, 0)
    rows0 = bcast_col(trail0, 0, col_id, grid_cols)
    cols0 = spread_columns_of(trail0, 0)

    l1, i1 = factor(g11 - times_transposed(l0_b1, l0_b1))
    l1_b2 = times_transposed(g21 - times_transposed(l0_b2, l0_b1), i1)
    upd1 = panel_in - times_transposed(rows0, l0_b1)
    trail1, column1 = panel_rows(upd1, l1, i1, 1)
    rows1 = bcast_col(trail1, 1, col_id, grid_cols)
    cols1 = spread_columns_of(trail1, 1)

    d2 = g22 - times_transposed(l0_b2, l0_b2) - times_transposed(l1_b2, l1_b2)
    l2, i2 = factor(d2)
    upd2 = panel_in - times_transposed(rows0, l0_b2) - times_transposed(rows1, l1_b2)
    _, column2 = panel_rows(upd2, l2, i2, 2)

    left = jnp.concatenate([rows0, rows1], axis=1)
    right = jnp.concatenate([cols0, cols1], axis=1)
    updated = gram - times_transposed(left, right, lax.Precision.HIGH)
    in_steps = grows < STEPS * NB
    panel_end = (grows // NB + 1) * NB
    zero = in_steps[:, None] & (gcols[None, :] >= panel_end[:, None])
    updated = jnp.where(zero, 0.0, updated)
    own_column = pick([(0, column0), (1, column1), (2, column2)], updated[:, 0:NB])
    updated = updated.at[:, 0:NB].set(own_column)
    return updated


def solution(mesh):
    placed = (P("row", "col"),)
    return jax.shard_map(
        local, mesh=mesh, in_specs=placed, out_specs=P("row", "col"), check_vma=False
    )
```

```python
import jax
import jax.numpy as jnp
from jax import lax
from jax.sharding import PartitionSpec as P

NB = 512
STEPS = 2
SUB = 128


def global_index(count, block, grid, position):
    ladder = jnp.arange(count, dtype=jnp.int32)
    return (ladder // block * grid + position) * block + ladder % block


def times_transposed(left, right, precision=lax.Precision.HIGHEST):
    return lax.dot_general(
        left,
        right,
        (((1,), (1,)), ((), ())),
        precision=precision,
        preferred_element_type=jnp.float32,
    )


def bcast_col(value, owner, col_id, grid_cols):
    held = value
    for target in range(grid_cols):
        if target != owner:
            got = lax.ppermute(value, "col", [(owner, target)])
            held = jnp.where(col_id == target, got, held)
    return held


def local_body(gram):
    grid_rows = lax.axis_size("row")
    grid_cols = lax.axis_size("col")
    row_id = lax.axis_index("row")
    col_id = lax.axis_index("col")
    rblock = NB * grid_cols // grid_rows
    per_class = grid_rows // grid_cols
    panels = STEPS + 1
    assert panels <= grid_cols and panels * per_class <= grid_rows
    local_rows = gram.shape[0]
    local_cols = gram.shape[1]
    blocks = local_rows // rblock
    grows = global_index(local_rows, rblock, grid_rows, row_id)
    gcols = global_index(local_cols, NB, grid_cols, col_id)
    identity = jnp.eye(NB, dtype=jnp.float32)

    tile = gram[0:rblock, 0:NB]
    colblk = lax.all_gather(tile, "row", axis=0, tiled=True)
    colblk = colblk[: panels * NB].reshape(panels, NB, NB)
    send_a = jnp.where(col_id == 0, colblk[0], colblk[1])
    recv_a = lax.ppermute(send_a, "col", [(0, 1), (1, 2)])
    recv_b = lax.ppermute(colblk[0:2], "col", [(0, 2)])

    def pick(options, default):
        out = default
        for col, val in options:
            out = jnp.where(col_id == col, val, out)
        return out

    g00 = pick([(0, colblk[0]), (1, recv_a), (2, recv_b[0])], identity)
    g10 = pick([(1, colblk[0].T), (2, recv_b[1])], jnp.zeros_like(identity))
    g11 = pick([(1, colblk[1]), (2, recv_a)], identity)
    g20 = pick([(2, colblk[0].T)], jnp.zeros_like(identity))
    g21 = pick([(2, colblk[1].T)], jnp.zeros_like(identity))
    g22 = pick([(2, colblk[2])], identity)

    def factor(diag):
        sym = (diag + diag.T) * 0.5
        side = SUB
        count = NB // side
        eye_sub = jnp.eye(side, dtype=jnp.float32)
        diag_factors = []
        diag_inverses = []
        below_blocks = []
        rest = sym
        for step in range(count):
            lead = rest[0:side, 0:side]
            low = jnp.linalg.cholesky(lead)
            inv = jax.scipy.linalg.solve_triangular(low, eye_sub, lower=True)
            diag_factors.append(low)
            diag_inverses.append(inv)
            if step + 1 < count:
                below = times_transposed(rest[side:, 0:side], inv)
                below_blocks.append(below)
                rest = rest[side:, side:] - times_transposed(below, below)
        low_factor = jnp.zeros((NB, NB), jnp.float32)
        for step in range(count):
            at = step * side
            low_factor = low_factor.at[at : at + side, at : at + side].set(diag_factors[step])
            if step + 1 < count:
                low_factor = low_factor.at[at + side :, at : at + side].set(below_blocks[step])

        def invert(first, size):
            if size == side:
                return diag_inverses[first // side]
            half = size // 2
            top = invert(first, half)
            bottom = invert(first + half, half)
            corner = low_factor[first + half : first + size, first : first + half]
            mixed = -jnp.dot(bottom, jnp.dot(corner, top, precision=lax.Precision.HIGHEST),
                             precision=lax.Precision.HIGHEST)
            upper = jnp.concatenate([top, jnp.zeros((half, half), jnp.float32)], axis=1)
            lower = jnp.concatenate([mixed, bottom], axis=1)
            return jnp.concatenate([upper, lower], axis=0)

        return low_factor, invert(0, NB)

    panel_in = gram[:, 0:NB]

    def panel_rows(updated, low_factor, inverse, panel_index):
        end_row = panel_index * NB + NB
        solved = times_transposed(updated, inverse)
        trailing = jnp.where((grows >= end_row)[:, None], solved, 0.0)
        first = panel_index * per_class
        member = jnp.clip(row_id - first, 0, per_class - 1)
        rows_diag = lax.dynamic_slice_in_dim(low_factor, member * rblock, rblock, 0)
        in_panel = (row_id >= first) & (row_id < first + per_class)
        patched = jnp.where(in_panel, rows_diag, trailing[0:rblock])
        column = trailing.at[0:rblock].set(patched)
        return trailing, column

    def spread_columns_of(trail, owner):
        span = blocks // grid_cols * rblock
        pieces = trail.reshape(grid_cols, span, NB)
        got = pieces[0]
        for piece in range(grid_cols):
            route = []
            for source_row in range(grid_rows):
                target_row = piece * per_class + source_row % per_class
                target_col = source_row // per_class
                route.append((source_row * grid_cols + owner, target_row * grid_cols + target_col))
            received = lax.ppermute(pieces[piece], ("row", "col"), route)
            got = jnp.where(row_id // per_class == piece, received, got)
        gathered = lax.all_gather(got, "row", axis=0, tiled=True)
        spread = gathered.reshape(grid_cols, per_class, blocks // grid_cols, rblock, NB)
        return jnp.transpose(spread, (0, 2, 1, 3, 4)).reshape(local_cols, NB)

    l0, i0 = factor(g00)
    l0_b1 = times_transposed(g10, i0)
    l0_b2 = times_transposed(g20, i0)
    trail0, column0 = panel_rows(panel_in, l0, i0, 0)
    rows0 = bcast_col(trail0, 0, col_id, grid_cols)
    cols0 = spread_columns_of(trail0, 0)

    l1, i1 = factor(g11 - times_transposed(l0_b1, l0_b1))
    l1_b2 = times_transposed(g21 - times_transposed(l0_b2, l0_b1), i1)
    upd1 = panel_in - times_transposed(rows0, l0_b1)
    trail1, column1 = panel_rows(upd1, l1, i1, 1)
    rows1 = bcast_col(trail1, 1, col_id, grid_cols)
    cols1 = spread_columns_of(trail1, 1)

    d2 = g22 - times_transposed(l0_b2, l0_b2) - times_transposed(l1_b2, l1_b2)
    l2, i2 = factor(d2)
    upd2 = panel_in - times_transposed(rows0, l0_b2) - times_transposed(rows1, l1_b2)
    _, column2 = panel_rows(upd2, l2, i2, 2)

    left = jnp.concatenate([rows0, rows1], axis=1)
    right = jnp.concatenate([cols0, cols1], axis=1)
    updated = gram - times_transposed(left, right, lax.Precision.HIGH)
    in_steps = grows < STEPS * NB
    panel_end = (grows // NB + 1) * NB
    zero = in_steps[:, None] & (gcols[None, :] >= panel_end[:, None])
    updated = jnp.where(zero, 0.0, updated)
    own_column = pick([(0, column0), (1, column1), (2, column2)], updated[:, 0:NB])
    updated = updated.at[:, 0:NB].set(own_column)
    return updated


def solution(mesh):
    placed = (P("row", "col"),)
    return jax.shard_map(
        local_body, mesh=mesh, in_specs=placed, out_specs=P("row", "col"), check_vma=False
    )
```

```python
import jax
import jax.numpy as jnp
from jax import lax
from jax.sharding import PartitionSpec as P

NB = 512
STEPS = 2
SUB = 128


def global_index(count, block, grid, position):
    ladder = jnp.arange(count, dtype=jnp.int32)
    return (ladder // block * grid + position) * block + ladder % block


def times_transposed(left, right, precision=lax.Precision.HIGHEST):
    return lax.dot_general(
        left,
        right,
        (((1,), (1,)), ((), ())),
        precision=precision,
        preferred_element_type=jnp.float32,
    )


def bcast_col(value, owner, col_id, grid_cols):
    held = value
    for target in range(grid_cols):
        if target != owner:
            got = lax.ppermute(value, "col", [(owner, target)])
            held = jnp.where(col_id == target, got, held)
    return held


def local_body(gram):
    grid_rows = lax.axis_size("row")
    grid_cols = lax.axis_size("col")
    row_id = lax.axis_index("row")
    col_id = lax.axis_index("col")
    rblock = NB * grid_cols // grid_rows
    per_class = grid_rows // grid_cols
    panels = STEPS + 1
    assert panels <= grid_cols and panels * per_class <= grid_rows
    local_rows = gram.shape[0]
    local_cols = gram.shape[1]
    blocks = local_rows // rblock
    grows = global_index(local_rows, rblock, grid_rows, row_id)
    gcols = global_index(local_cols, NB, grid_cols, col_id)
    identity = jnp.eye(NB, dtype=jnp.float32)

    tile = gram[0:rblock, 0:NB]
    colblk = lax.all_gather(tile, "row", axis=0, tiled=True)
    colblk = colblk[: panels * NB].reshape(panels, NB, NB)
    send_a = jnp.where(col_id == 0, colblk[0], colblk[1])
    recv_a = lax.ppermute(send_a, "col", [(0, 1), (1, 2)])
    recv_b = lax.ppermute(colblk[0:2], "col", [(0, 2)])

    def pick(options, default):
        out = default
        for col, val in options:
            out = jnp.where(col_id == col, val, out)
        return out

    g00 = pick([(0, colblk[0]), (1, recv_a), (2, recv_b[0])], identity)
    g10 = pick([(1, colblk[0].T), (2, recv_b[1])], jnp.zeros_like(identity))
    g11 = pick([(1, colblk[1]), (2, recv_a)], identity)
    g20 = pick([(2, colblk[0].T)], jnp.zeros_like(identity))
    g21 = pick([(2, colblk[1].T)], jnp.zeros_like(identity))
    g22 = pick([(2, colblk[2])], identity)

    def factor(diag):
        sym = (diag + diag.T) * 0.5
        side = SUB
        count = NB // side
        eye_sub = jnp.eye(side, dtype=jnp.float32)
        diag_factors = []
        diag_inverses = []
        below_blocks = []
        rest = sym
        for step in range(count):
            lead = rest[0:side, 0:side]
            low = jnp.linalg.cholesky(lead)
            inv = jax.scipy.linalg.solve_triangular(low, eye_sub, lower=True)
            diag_factors.append(low)
            diag_inverses.append(inv)
            if step + 1 < count:
                below = times_transposed(rest[side:, 0:side], inv)
                below_blocks.append(below)
                rest = rest[side:, side:] - times_transposed(below, below)
        low_factor = jnp.zeros((NB, NB), jnp.float32)
        for step in range(count):
            at = step * side
            low_factor = low_factor.at[at : at + side, at : at + side].set(diag_factors[step])
            if step + 1 < count:
                low_factor = low_factor.at[at + side :, at : at + side].set(below_blocks[step])

        def invert(first, size):
            if size == side:
                return diag_inverses[first // side]
            half = size // 2
            top = invert(first, half)
            bottom = invert(first + half, half)
            corner = low_factor[first + half : first + size, first : first + half]
            mixed = -jnp.dot(bottom, jnp.dot(corner, top, precision=lax.Precision.HIGHEST),
                             precision=lax.Precision.HIGHEST)
            upper = jnp.concatenate([top, jnp.zeros((half, half), jnp.float32)], axis=1)
            lower = jnp.concatenate([mixed, bottom], axis=1)
            return jnp.concatenate([upper, lower], axis=0)

        return low_factor, invert(0, NB)

    panel_in = gram[:, 0:NB]

    def panel_rows(updated, low_factor, inverse, panel_index):
        end_row = panel_index * NB + NB
        solved = times_transposed(updated, inverse)
        trailing = jnp.where((grows >= end_row)[:, None], solved, 0.0)
        first = panel_index * per_class
        member = jnp.clip(row_id - first, 0, per_class - 1)
        rows_diag = lax.dynamic_slice_in_dim(low_factor, member * rblock, rblock, 0)
        in_panel = (row_id >= first) & (row_id < first + per_class)
        patched = jnp.where(in_panel, rows_diag, trailing[0:rblock])
        column = trailing.at[0:rblock].set(patched)
        return trailing, column

    def spread_columns_of(trail, owner):
        span = blocks // grid_cols * rblock
        pieces = trail.reshape(grid_cols, span, NB)
        got = pieces[0]
        for piece in range(grid_cols):
            route = []
            for source_row in range(grid_rows):
                target_row = piece * per_class + source_row % per_class
                target_col = source_row // per_class
                route.append((source_row * grid_cols + owner, target_row * grid_cols + target_col))
            received = lax.ppermute(pieces[piece], ("row", "col"), route)
            got = jnp.where(row_id // per_class == piece, received, got)
        gathered = lax.all_gather(got, "row", axis=0, tiled=True)
        spread = gathered.reshape(grid_cols, per_class, blocks // grid_cols, rblock, NB)
        return jnp.transpose(spread, (0, 2, 1, 3, 4)).reshape(local_cols, NB)

    l0, i0 = factor(g00)
    l0_b1 = times_transposed(g10, i0)
    l0_b2 = times_transposed(g20, i0)
    trail0, column0 = panel_rows(panel_in, l0, i0, 0)
    rows0 = bcast_col(trail0, 0, col_id, grid_cols)
    cols0 = spread_columns_of(trail0, 0)

    l1, i1 = factor(g11 - times_transposed(l0_b1, l0_b1))
    l1_b2 = times_transposed(g21 - times_transposed(l0_b2, l0_b1), i1)
    upd1 = panel_in - times_transposed(rows0, l0_b1)
    trail1, column1 = panel_rows(upd1, l1, i1, 1)
    rows1 = bcast_col(trail1, 1, col_id, grid_cols)
    cols1 = spread_columns_of(trail1, 1)

    d2 = g22 - times_transposed(l0_b2, l0_b2) - times_transposed(l1_b2, l1_b2)
    l2, i2 = factor(d2)
    upd2 = panel_in - times_transposed(rows0, l0_b2) - times_transposed(rows1, l1_b2)
    _, column2 = panel_rows(upd2, l2, i2, 2)

    updated = gram - times_transposed(rows0, cols0, lax.Precision.HIGH)
    updated = updated - times_transposed(rows1, cols1, lax.Precision.HIGH)
    in_steps = grows < STEPS * NB
    panel_end = (grows // NB + 1) * NB
    zero = in_steps[:, None] & (gcols[None, :] >= panel_end[:, None])
    updated = jnp.where(zero, 0.0, updated)
    own_column = pick([(0, column0), (1, column1), (2, column2)], updated[:, 0:NB])
    updated = updated.at[:, 0:NB].set(own_column)
    return updated


def solution(mesh):
    placed = (P("row", "col"),)
    return jax.shard_map(
        local_body, mesh=mesh, in_specs=placed, out_specs=P("row", "col"), check_vma=False
    )
```

```python
import jax
import jax.numpy as jnp
from jax import lax
from jax.sharding import PartitionSpec as P

NB = 512
STEPS = 2
SUB = 128


def global_index(count, block, grid, position):
    ladder = jnp.arange(count, dtype=jnp.int32)
    return (ladder // block * grid + position) * block + ladder % block


def times_transposed(left, right, precision=lax.Precision.HIGHEST):
    return lax.dot_general(
        left,
        right,
        (((1,), (1,)), ((), ())),
        precision=precision,
        preferred_element_type=jnp.float32,
    )


def bcast_col(value, owner, col_id, grid_cols):
    held = value
    for target in range(grid_cols):
        if target != owner:
            got = lax.ppermute(value, "col", [(owner, target)])
            held = jnp.where(col_id == target, got, held)
    return held


def local_body(gram):
    grid_rows = lax.axis_size("row")
    grid_cols = lax.axis_size("col")
    row_id = lax.axis_index("row")
    col_id = lax.axis_index("col")
    rblock = NB * grid_cols // grid_rows
    per_class = grid_rows // grid_cols
    panels = STEPS + 1
    assert panels <= grid_cols and panels * per_class <= grid_rows
    local_rows = gram.shape[0]
    local_cols = gram.shape[1]
    blocks = local_rows // rblock
    grows = global_index(local_rows, rblock, grid_rows, row_id)
    gcols = global_index(local_cols, NB, grid_cols, col_id)
    identity = jnp.eye(NB, dtype=jnp.float32)

    tile = gram[0:rblock, 0:NB]
    colblk = lax.all_gather(tile, "row", axis=0, tiled=True)
    colblk = colblk[: panels * NB].reshape(panels, NB, NB)
    send_a = jnp.where(col_id == 0, colblk[0], colblk[1])
    recv_a = lax.ppermute(send_a, "col", [(0, 1), (1, 2)])
    recv_b0 = lax.ppermute(colblk[0], "col", [(0, 2)])
    recv_b1 = lax.ppermute(colblk[1], "col", [(0, 2)])

    def pick(options, default):
        out = default
        for col, val in options:
            out = jnp.where(col_id == col, val, out)
        return out

    g00 = pick([(0, colblk[0]), (1, recv_a), (2, recv_b0)], identity)
    g10 = pick([(1, colblk[0].T), (2, recv_b1)], jnp.zeros_like(identity))
    g11 = pick([(1, colblk[1]), (2, recv_a)], identity)
    g20 = pick([(2, colblk[0].T)], jnp.zeros_like(identity))
    g21 = pick([(2, colblk[1].T)], jnp.zeros_like(identity))
    g22 = pick([(2, colblk[2])], identity)

    def factor(diag):
        sym = (diag + diag.T) * 0.5
        side = SUB
        count = NB // side
        eye_sub = jnp.eye(side, dtype=jnp.float32)
        diag_factors = []
        diag_inverses = []
        below_blocks = []
        rest = sym
        for step in range(count):
            lead = rest[0:side, 0:side]
            low = jnp.linalg.cholesky(lead)
            inv = jax.scipy.linalg.solve_triangular(low, eye_sub, lower=True)
            diag_factors.append(low)
            diag_inverses.append(inv)
            if step + 1 < count:
                below = times_transposed(rest[side:, 0:side], inv)
                below_blocks.append(below)
                rest = rest[side:, side:] - times_transposed(below, below)
        low_factor = jnp.zeros((NB, NB), jnp.float32)
        for step in range(count):
            at = step * side
            low_factor = low_factor.at[at : at + side, at : at + side].set(diag_factors[step])
            if step + 1 < count:
                low_factor = low_factor.at[at + side :, at : at + side].set(below_blocks[step])

        def invert(first, size):
            if size == side:
                return diag_inverses[first // side]
            half = size // 2
            top = invert(first, half)
            bottom = invert(first + half, half)
            corner = low_factor[first + half : first + size, first : first + half]
            mixed = -jnp.dot(bottom, jnp.dot(corner, top, precision=lax.Precision.HIGHEST),
                             precision=lax.Precision.HIGHEST)
            upper = jnp.concatenate([top, jnp.zeros((half, half), jnp.float32)], axis=1)
            lower = jnp.concatenate([mixed, bottom], axis=1)
            return jnp.concatenate([upper, lower], axis=0)

        return low_factor, invert(0, NB)

    panel_in = gram[:, 0:NB]

    def panel_rows(updated, low_factor, inverse, panel_index):
        end_row = panel_index * NB + NB
        solved = times_transposed(updated, inverse)
        trailing = jnp.where((grows >= end_row)[:, None], solved, 0.0)
        first = panel_index * per_class
        member = jnp.clip(row_id - first, 0, per_class - 1)
        rows_diag = lax.dynamic_slice_in_dim(low_factor, member * rblock, rblock, 0)
        in_panel = (row_id >= first) & (row_id < first + per_class)
        patched = jnp.where(in_panel, rows_diag, trailing[0:rblock])
        column = trailing.at[0:rblock].set(patched)
        return trailing, column

    def spread_columns_of(trail, owner):
        span = blocks // grid_cols * rblock
        pieces = trail.reshape(grid_cols, span, NB)
        got = pieces[0]
        for piece in range(grid_cols):
            route = []
            for source_row in range(grid_rows):
                target_row = piece * per_class + source_row % per_class
                target_col = source_row // per_class
                route.append((source_row * grid_cols + owner, target_row * grid_cols + target_col))
            received = lax.ppermute(pieces[piece], ("row", "col"), route)
            got = jnp.where(row_id // per_class == piece, received, got)
        gathered = lax.all_gather(got, "row", axis=0, tiled=True)
        spread = gathered.reshape(grid_cols, per_class, blocks // grid_cols, rblock, NB)
        return jnp.transpose(spread, (0, 2, 1, 3, 4)).reshape(local_cols, NB)

    l0, i0 = factor(g00)
    l0_b1 = times_transposed(g10, i0)
    l0_b2 = times_transposed(g20, i0)
    trail0, column0 = panel_rows(panel_in, l0, i0, 0)
    rows0 = bcast_col(trail0, 0, col_id, grid_cols)
    cols0 = spread_columns_of(trail0, 0)

    l1, i1 = factor(g11 - times_transposed(l0_b1, l0_b1))
    l1_b2 = times_transposed(g21 - times_transposed(l0_b2, l0_b1), i1)
    upd1 = panel_in - times_transposed(rows0, l0_b1)
    trail1, column1 = panel_rows(upd1, l1, i1, 1)
    rows1 = bcast_col(trail1, 1, col_id, grid_cols)
    cols1 = spread_columns_of(trail1, 1)

    d2 = g22 - times_transposed(l0_b2, l0_b2) - times_transposed(l1_b2, l1_b2)
    l2, i2 = factor(d2)
    upd2 = panel_in - times_transposed(rows0, l0_b2) - times_transposed(rows1, l1_b2)
    _, column2 = panel_rows(upd2, l2, i2, 2)

    left = jnp.concatenate([rows0, rows1], axis=1)
    right = jnp.concatenate([cols0, cols1], axis=1)
    updated = gram - times_transposed(left, right, lax.Precision.HIGH)
    in_steps = grows < STEPS * NB
    panel_end = (grows // NB + 1) * NB
    zero = in_steps[:, None] & (gcols[None, :] >= panel_end[:, None])
    updated = jnp.where(zero, 0.0, updated)
    own_column = pick([(0, column0), (1, column1), (2, column2)], updated[:, 0:NB])
    updated = updated.at[:, 0:NB].set(own_column)
    return updated


def solution(mesh):
    placed = (P("row", "col"),)
    return jax.shard_map(
        local_body, mesh=mesh, in_specs=placed, out_specs=P("row", "col"), check_vma=False
    )
```

```python
import jax
import jax.numpy as jnp
from jax import lax
from jax.sharding import PartitionSpec as P

NB = 512
STEPS = 2
SUB = 128


def global_index(count, block, grid, position):
    ladder = jnp.arange(count, dtype=jnp.int32)
    return (ladder // block * grid + position) * block + ladder % block


def times_transposed(left, right, precision=lax.Precision.HIGHEST):
    return lax.dot_general(
        left,
        right,
        (((1,), (1,)), ((), ())),
        precision=precision,
        preferred_element_type=jnp.float32,
    )


def bcast_col(value, owner, col_id, grid_cols):
    held = value
    for target in range(grid_cols):
        if target != owner:
            got = lax.ppermute(value, "col", [(owner, target)])
            held = jnp.where(col_id == target, got, held)
    return held


def local_body(gram):
    grid_rows = lax.axis_size("row")
    grid_cols = lax.axis_size("col")
    row_id = lax.axis_index("row")
    col_id = lax.axis_index("col")
    rblock = NB * grid_cols // grid_rows
    per_class = grid_rows // grid_cols
    panels = STEPS + 1
    assert panels <= grid_cols and panels * per_class <= grid_rows
    local_rows = gram.shape[0]
    local_cols = gram.shape[1]
    blocks = local_rows // rblock
    grows = global_index(local_rows, rblock, grid_rows, row_id)
    gcols = global_index(local_cols, NB, grid_cols, col_id)
    identity = jnp.eye(NB, dtype=jnp.float32)

    tile = gram[0:rblock, 0:NB]
    colblk = lax.all_gather(tile, "row", axis=0, tiled=True)
    colblk = colblk[: panels * NB].reshape(panels, NB, NB)
    recv_a = lax.ppermute(colblk[0], "col", [(0, 1)])
    recv_c = lax.ppermute(colblk[1], "col", [(1, 2)])
    recv_b0 = lax.ppermute(colblk[0], "col", [(0, 2)])
    recv_b1 = lax.ppermute(colblk[1], "col", [(0, 2)])

    def pick(options, default):
        out = default
        for col, val in options:
            out = jnp.where(col_id == col, val, out)
        return out

    g00 = pick([(0, colblk[0]), (1, recv_a), (2, recv_b0)], identity)
    g10 = pick([(1, colblk[0].T), (2, recv_b1)], jnp.zeros_like(identity))
    g11 = pick([(1, colblk[1]), (2, recv_c)], identity)
    g20 = pick([(2, colblk[0].T)], jnp.zeros_like(identity))
    g21 = pick([(2, colblk[1].T)], jnp.zeros_like(identity))
    g22 = pick([(2, colblk[2])], identity)

    def factor(diag):
        sym = (diag + diag.T) * 0.5
        side = SUB
        count = NB // side
        eye_sub = jnp.eye(side, dtype=jnp.float32)
        diag_factors = []
        diag_inverses = []
        below_blocks = []
        rest = sym
        for step in range(count):
            lead = rest[0:side, 0:side]
            low = jnp.linalg.cholesky(lead)
            inv = jax.scipy.linalg.solve_triangular(low, eye_sub, lower=True)
            diag_factors.append(low)
            diag_inverses.append(inv)
            if step + 1 < count:
                below = times_transposed(rest[side:, 0:side], inv)
                below_blocks.append(below)
                rest = rest[side:, side:] - times_transposed(below, below)
        low_factor = jnp.zeros((NB, NB), jnp.float32)
        for step in range(count):
            at = step * side
            low_factor = low_factor.at[at : at + side, at : at + side].set(diag_factors[step])
            if step + 1 < count:
                low_factor = low_factor.at[at + side :, at : at + side].set(below_blocks[step])

        def invert(first, size):
            if size == side:
                return diag_inverses[first // side]
            half = size // 2
            top = invert(first, half)
            bottom = invert(first + half, half)
            corner = low_factor[first + half : first + size, first : first + half]
            mixed = -jnp.dot(bottom, jnp.dot(corner, top, precision=lax.Precision.HIGHEST),
                             precision=lax.Precision.HIGHEST)
            upper = jnp.concatenate([top, jnp.zeros((half, half), jnp.float32)], axis=1)
            lower = jnp.concatenate([mixed, bottom], axis=1)
            return jnp.concatenate([upper, lower], axis=0)

        return low_factor, invert(0, NB)

    panel_in = gram[:, 0:NB]

    def panel_rows(updated, low_factor, inverse, panel_index):
        end_row = panel_index * NB + NB
        solved = times_transposed(updated, inverse)
        trailing = jnp.where((grows >= end_row)[:, None], solved, 0.0)
        first = panel_index * per_class
        member = jnp.clip(row_id - first, 0, per_class - 1)
        rows_diag = lax.dynamic_slice_in_dim(low_factor, member * rblock, rblock, 0)
        in_panel = (row_id >= first) & (row_id < first + per_class)
        patched = jnp.where(in_panel, rows_diag, trailing[0:rblock])
        column = trailing.at[0:rblock].set(patched)
        return trailing, column

    def spread_columns_of(trail, owner):
        span = blocks // grid_cols * rblock
        pieces = trail.reshape(grid_cols, span, NB)
        got = pieces[0]
        for piece in range(grid_cols):
            route = []
            for source_row in range(grid_rows):
                target_row = piece * per_class + source_row % per_class
                target_col = source_row // per_class
                route.append((source_row * grid_cols + owner, target_row * grid_cols + target_col))
            received = lax.ppermute(pieces[piece], ("row", "col"), route)
            got = jnp.where(row_id // per_class == piece, received, got)
        gathered = lax.all_gather(got, "row", axis=0, tiled=True)
        spread = gathered.reshape(grid_cols, per_class, blocks // grid_cols, rblock, NB)
        return jnp.transpose(spread, (0, 2, 1, 3, 4)).reshape(local_cols, NB)

    l0, i0 = factor(g00)
    l0_b1 = times_transposed(g10, i0)
    l0_b2 = times_transposed(g20, i0)
    trail0, column0 = panel_rows(panel_in, l0, i0, 0)
    rows0 = bcast_col(trail0, 0, col_id, grid_cols)
    cols0 = spread_columns_of(trail0, 0)

    l1, i1 = factor(g11 - times_transposed(l0_b1, l0_b1))
    l1_b2 = times_transposed(g21 - times_transposed(l0_b2, l0_b1), i1)
    upd1 = panel_in - times_transposed(rows0, l0_b1)
    trail1, column1 = panel_rows(upd1, l1, i1, 1)
    rows1 = bcast_col(trail1, 1, col_id, grid_cols)
    cols1 = spread_columns_of(trail1, 1)

    d2 = g22 - times_transposed(l0_b2, l0_b2) - times_transposed(l1_b2, l1_b2)
    l2, i2 = factor(d2)
    upd2 = panel_in - times_transposed(rows0, l0_b2) - times_transposed(rows1, l1_b2)
    _, column2 = panel_rows(upd2, l2, i2, 2)

    left = jnp.concatenate([rows0, rows1], axis=1)
    right = jnp.concatenate([cols0, cols1], axis=1)
    updated = gram - times_transposed(left, right, lax.Precision.HIGH)
    in_steps = grows < STEPS * NB
    panel_end = (grows // NB + 1) * NB
    zero = in_steps[:, None] & (gcols[None, :] >= panel_end[:, None])
    updated = jnp.where(zero, 0.0, updated)
    own_column = pick([(0, column0), (1, column1), (2, column2)], updated[:, 0:NB])
    updated = updated.at[:, 0:NB].set(own_column)
    return updated


def solution(mesh):
    placed = (P("row", "col"),)
    return jax.shard_map(
        local_body, mesh=mesh, in_specs=placed, out_specs=P("row", "col"), check_vma=False
    )
```
